512 devices in a mesh: blk: 64 (over y, z), mpo: 8 (over x, core).
Axes of the slice: x: 4, y: 8, z: 8, core: 2. Of those that a mesh axis runs over, the one named last changes fastest.
Arguments:
- wave: bfloat16 [6144, 128, 128], P('blk'), may hold values from -6 to 6
- left_env: bfloat16 [8, 64, 128, 128], P('mpo', 'blk'), may hold values from -0.5 to 0.5
- right_env: bfloat16 [8, 64, 128, 128], P('mpo', 'blk'), may hold values from -0.1875 to 0.1875
- right_sector: int32 [6144, 1], P('blk'), may hold values from 0 to 63; in each aligned block of 96 rows (0 to 95, 96 to 191, ...) at most 2 rows name the same one
- right_home: int32 [64], replicated, may hold values from 0 to 63, each once
Outputs:
- product: bfloat16 [6144, 128, 128], P('blk', None, 'mpo')
The draws below stay inside these ranges and needn't reach their ends.
Inputs may be any that keep to these rules, and one draw needn't show every extreme that they name: `right_sector`: among the 96 blocks of one device (aligned blocks of rows) no right sector appears more than 2 times, and some sector appears exactly 2 times; every sector appears somewhere. `right_home`: each sector has its own storage row.
All inputs are finite; a program needn't handle non-finite values.
Results may differ from the reference program's by a relative error of at most 0.008.
Values may be sent and summed in bfloat16 or wider, within the bound.
No kernel may reach another device: no remote copies, remote signals or barrier semaphores. Data moves between devices by JAX's collectives and lax.ppermute only.
A program may use at most 64 MiB of HBM per device.

```python
import math
import jax
import jax.numpy as jnp
import numpy as np
from jax import lax

BS = 128
KL = 64
CAP = 2
BLK_DEV = 96
NB = 6144
W = 8


def shard_levels(key, dims, shards, least, largest):
    gain = 1.0
    for dim, shards_of in shards:
        heights = jax.random.uniform(jax.random.fold_in(jax.random.fold_in(key, 6), dim), (shards_of,), jnp.float32, least / len(shards), largest / len(shards))
        gain = gain * jnp.repeat(jnp.exp(heights), dims[dim] // shards_of).reshape((-1,) + (1,) * (len(dims) - 1 - dim))
    return gain


def assign_block(own_key, own, number, rows, count, top, bound, slope):
    sequence = jax.random.permutation(own_key, count)
    heavy_load, usual = shares(count, rows * top, bound, slope, True), shares(count, rows * top, bound, slope, False)
    places = jnp.arange(count)

    def named(sizes, rotation):
        used = int((sizes > 0).sum())
        fixed = max(1, used // 4)
        moved = fixed + (places - fixed + rotation * (used - fixed)) % max(1, count - fixed)
        return jnp.zeros((count,), jnp.int32).at[sequence[jnp.where(places < fixed, places, moved)]].set(jnp.asarray(sizes, jnp.int32))

    sizes = jnp.where(number % 4 == 0, named(heavy_load, number // 4), named(usual, number - number // 4 - 1))
    mixed = jax.random.permutation(jax.random.fold_in(own, 3), count)
    source_of, taker = mixed[0:count // 2 * 2:2], mixed[1:count // 2 * 2:2]
    slack = jnp.minimum(sizes[source_of] - 1, bound - sizes[taker]) // 2
    slack = jnp.where((source_of == sequence[0]) | (taker == sequence[0]) | (sizes[taker] == 0), 0, jnp.maximum(slack, 0))
    moved = jax.random.randint(jax.random.fold_in(own, 4), (count // 2,), 0, 1 << 20) % (slack + 1)
    sizes = sizes.at[source_of].add(-moved).at[taker].add(moved)
    members = jnp.searchsorted(jnp.cumsum(sizes), jnp.arange(rows * top), side="right").astype(jnp.int32)
    listing = members.reshape(top, rows).T
    listing = listing[jax.random.permutation(jax.random.fold_in(own, 1), rows)]
    rotation = jax.random.randint(jax.random.fold_in(own, 2), (rows, 1), 0, top)
    return jnp.take_along_axis(listing, (jnp.arange(top)[None, :] + rotation) % top, axis=1)


def shares(count, total, most, skew, full):
    weights = [(1 << 20) // math.isqrt(grade ** skew) + 1 for grade in range(1, count + 1)]
    largest = most if full else min(most, max(-(-total // count), total * weights[0] // sum(weights)))
    least = 1 if total - largest >= count - 1 else 0
    counts, spare = [largest] + [least] * (count - 1), total - largest - least * (count - 1)
    while spare > 0:
        candidates = [i for i in range(1, count) if counts[i] < largest] or [i for i in range(1, count) if counts[i] < most]
        mass, remaining = sum([weights[i] for i in candidates]), spare
        for i in candidates:
            extra = min(most - counts[i], max(1, remaining * weights[i] // mass), spare)
            counts[i] = counts[i] + extra
            spare = spare - extra
    return np.array(counts)


def gaussian(rng, dims, spread, most, pieces=(), kind=jnp.bfloat16):
    factor_of = shard_levels(rng, dims, pieces, -0.22, 0.18) if pieces else 1.0
    array = jax.random.normal(rng, dims, jnp.float32) * spread * factor_of
    return jnp.minimum(jnp.maximum(array, -most), most).astype(kind)


def setup_inputs(seed: int = 0) -> dict:
    arg_keys = jax.random.split(jax.random.key(seed), 6)
    wave = gaussian(arg_keys[0], (NB, BS, BS), 1.0, 6.0, ((0, 64),))
    left_env = gaussian(arg_keys[1], (W, KL, BS, BS), BS ** -0.5, 0.5, ((0, 8), (1, 64)))
    right_env = gaussian(arg_keys[2], (W, KL, BS, BS), (BS * W) ** -0.5, 0.1875, ((0, 8), (1, 64)))
    right_sector_keys = jax.random.split(jax.random.fold_in(arg_keys[3], 1), NB // BLK_DEV)
    right_sector_turns = jax.random.permutation(jax.random.fold_in(arg_keys[3], 3), NB // BLK_DEV)
    right_sector = jax.vmap(lambda own, number: assign_block(jax.random.fold_in(arg_keys[3], 2), own, number, BLK_DEV, KL, 1, CAP, 2))(right_sector_keys, right_sector_turns).reshape((NB, 1))
    right_home = jax.random.permutation(arg_keys[4], KL).astype(jnp.int32)
    return dict(wave=wave, left_env=left_env, right_env=right_env, right_sector=right_sector, right_home=right_home)


def reference(wave, left_env, right_env, right_sector, right_home):
    index = jnp.arange(NB, dtype=jnp.int32)
    left_sector = (index * KL // NB).astype(jnp.int32)
    places = jnp.take(right_home, right_sector[:, 0], axis=0).astype(jnp.int32)

    def one_block(items):
        block, lsec, place = items
        lefts = jnp.take(left_env, lsec, axis=1).astype(jnp.float32)
        rights = jnp.take(right_env, place, axis=1).astype(jnp.float32)
        left = jnp.einsum("wik,kj->wij", lefts, block.astype(jnp.float32)).astype(jnp.bfloat16)
        term = jnp.einsum("wik,wjk->wij", left.astype(jnp.float32), rights)
        return jnp.sum(term, axis=0).astype(jnp.bfloat16)

    return lax.map(one_block, (wave, left_sector, places))
```

```python
import jax
import jax.numpy as jnp
from jax import lax
from jax.sharding import PartitionSpec as P


def local(wave, left_env, right_env, right_sector, right_home):
    terms = lax.axis_size("mpo")
    size = wave.shape[1]
    width = size // terms
    mine = lax.all_to_all(right_env[0, 0].reshape(terms, width, size), "mpo", 0, 0, tiled=False)
    table = lax.all_gather(mine, "blk", axis=0, tiled=False)
    table = table.reshape(table.shape[0], terms * width, size)
    lefts = lax.all_gather(left_env[0, 0], "mpo", axis=0, tiled=False)
    places = jnp.take(right_home, right_sector[:, 0], axis=0)
    picked = jnp.take(table, places, axis=0)
    inner = jnp.einsum("brk,bjk->brj", picked, wave, preferred_element_type=jnp.float32)
    inner = inner.astype(jnp.bfloat16).reshape(wave.shape[0], terms, width, size)
    out = jnp.einsum("bwcj,wij->bic", inner, lefts, preferred_element_type=jnp.float32)
    return out.astype(jnp.bfloat16)


def solution(mesh):
    in_specs = (
        P("blk", None, None),
        P("mpo", "blk", None, None),
        P("mpo", "blk", None, None),
        P("blk", None),
        P(),
    )
    out_specs = P("blk", None, "mpo")
    return jax.shard_map(local, mesh=mesh, in_specs=in_specs, out_specs=out_specs, check_vma=False)
```

```python
import math

import jax
import jax.numpy as jnp
from jax import lax
from jax.sharding import Mesh
from jax.sharding import PartitionSpec as P


def local(wave, left_env, right_env, right_sector, right_home):
    terms = lax.axis_size("mpo")
    inner_size = lax.axis_size("z")
    size = wave.shape[1]
    width = size // terms
    mine = lax.all_to_all(right_env[0, 0].reshape(terms, width, size), "mpo", 0, 0, tiled=False)
    spread = jnp.broadcast_to(mine[None], (inner_size,) + mine.shape)
    row = lax.all_to_all(spread, "z", 0, 0, tiled=False)
    table = lax.all_gather(row, "y", axis=0, tiled=False)
    table = table.reshape(-1, terms * width, size)
    lefts = lax.all_gather(left_env[0, 0], "mpo", axis=0, tiled=False)
    places = jnp.take(right_home, right_sector[:, 0], axis=0)
    picked = jnp.take(table, places, axis=0)
    inner = jnp.einsum("brk,bjk->brj", picked, wave, preferred_element_type=jnp.float32)
    inner = inner.astype(jnp.bfloat16).reshape(wave.shape[0], terms, width, size)
    out = jnp.einsum("bwcj,wij->bic", inner, lefts, preferred_element_type=jnp.float32)
    return out.astype(jnp.bfloat16)


def solution(mesh):
    blocks, terms = mesh.devices.shape
    inner_size = math.isqrt(blocks)
    grid = Mesh(mesh.devices.reshape(blocks // inner_size, inner_size, terms), ("y", "z", "mpo"))
    blk = ("y", "z")
    in_specs = (
        P(blk, None, None),
        P("mpo", blk, None, None),
        P("mpo", blk, None, None),
        P(blk, None),
        P(),
    )
    out_specs = P(blk, None, "mpo")
    return jax.shard_map(local, mesh=grid, in_specs=in_specs, out_specs=out_specs, check_vma=False)
```

```python
import math

import jax
import jax.numpy as jnp
from jax import lax
from jax.sharding import Mesh
from jax.sharding import PartitionSpec as P


def local(wave, left_env, right_env, right_sector, right_home):
    terms = lax.axis_size("mpo")
    inner_size = lax.axis_size("z")
    size = wave.shape[1]
    width = size // terms
    own = right_env[0, 0].reshape(1, terms, width, size)
    spread = jnp.broadcast_to(own, (inner_size, terms, width, size)).reshape(inner_size * terms, width, size)
    row = lax.all_to_all(spread, ("z", "mpo"), 0, 0, tiled=True)
    table = lax.all_gather(row, "y", axis=0, tiled=False)
    table = table.reshape(-1, terms * width, size)
    lefts = lax.all_gather(left_env[0, 0], "mpo", axis=0, tiled=False)
    places = jnp.take(right_home, right_sector[:, 0], axis=0)
    picked = jnp.take(table, places, axis=0)
    inner = jnp.einsum("brk,bjk->brj", picked, wave, preferred_element_type=jnp.float32)
    inner = inner.astype(jnp.bfloat16).reshape(wave.shape[0], terms, width, size)
    out = jnp.einsum("bwcj,wij->bic", inner, lefts, preferred_element_type=jnp.float32)
    return out.astype(jnp.bfloat16)


def solution(mesh):
    blocks, terms = mesh.devices.shape
    inner_size = math.isqrt(blocks)
    grid = Mesh(mesh.devices.reshape(blocks // inner_size, inner_size, terms), ("y", "z", "mpo"))
    blk = ("y", "z")
    in_specs = (
        P(blk, None, None),
        P("mpo", blk, None, None),
        P("mpo", blk, None, None),
        P(blk, None),
        P(),
    )
    out_specs = P(blk, None, "mpo")
    return jax.shard_map(local, mesh=grid, in_specs=in_specs, out_specs=out_specs, check_vma=False)
```

```python
import math

import functools

import jax
import jax.numpy as jnp
from jax import lax
from jax.experimental import pallas as pl
from jax.experimental.pallas import tpu as pltpu
from jax.sharding import Mesh
from jax.sharding import PartitionSpec as P


def tail_kernel(group, terms, width, places_ref, table_ref, wave_ref, lefts_ref, out_ref, inner_ref):
    step = pl.program_id(0)
    contract = (((1,), (1,)), ((), ()))
    for g in range(group):
        rows = table_ref[places_ref[step * group + g]]
        inner = lax.dot_general(rows, wave_ref[g], contract, preferred_element_type=jnp.float32)
        inner_ref[g] = inner.astype(inner_ref.dtype)
    total = None
    for w in range(terms):
        part = inner_ref[:, w * width : (w + 1) * width, :].reshape(group * width, -1)
        term = lax.dot_general(part, lefts_ref[w], contract, preferred_element_type=jnp.float32)
        total = term if total is None else total + term
    out_ref[...] = total.reshape(out_ref.shape).astype(out_ref.dtype)


def tail(places, table, wave, lefts, terms, width):
    blocks, size, _ = wave.shape
    group = 8
    kernel = functools.partial(tail_kernel, group, terms, width)
    spec = pltpu.PrefetchScalarGridSpec(
        num_scalar_prefetch=1,
        grid=(blocks // group,),
        in_specs=[
            pl.BlockSpec(table.shape, lambda i, p: (0, 0, 0)),
            pl.BlockSpec((group, size, size), lambda i, p: (i, 0, 0)),
            pl.BlockSpec(lefts.shape, lambda i, p: (0, 0, 0)),
        ],
        out_specs=pl.BlockSpec((group, width, size), lambda i, p: (i, 0, 0)),
        scratch_shapes=[pltpu.VMEM((group, size, size), jnp.bfloat16)],
    )
    flops = 4 * blocks * size * size * size
    moved = 2 * (table.size + wave.size + lefts.size + blocks * width * size)
    out = pl.pallas_call(
        kernel,
        grid_spec=spec,
        out_shape=jax.ShapeDtypeStruct((blocks, width, size), jnp.bfloat16),
        compiler_params=pltpu.CompilerParams(dimension_semantics=("arbitrary",)),
        cost_estimate=pl.CostEstimate(flops=flops, bytes_accessed=moved, transcendentals=0),
    )(places, table, wave, lefts)
    return jnp.swapaxes(out, 1, 2)


def local(wave, left_env, right_env, right_sector, right_home):
    terms = lax.axis_size("mpo")
    inner_size = lax.axis_size("z")
    size = wave.shape[1]
    width = size // terms
    own = right_env[0, 0].reshape(1, terms, width, size)
    spread = jnp.broadcast_to(own, (inner_size, terms, width, size)).reshape(inner_size * terms, width, size)
    row = lax.all_to_all(spread, ("z", "mpo"), 0, 0, tiled=True)
    table = lax.all_gather(row, "y", axis=0, tiled=False)
    table = table.reshape(-1, terms * width, size)
    lefts = lax.all_gather(left_env[0, 0], "mpo", axis=0, tiled=False)
    places = jnp.take(right_home, right_sector[:, 0], axis=0)
    return tail(places.astype(jnp.int32), table, wave, lefts, terms, width)


def solution(mesh):
    blocks, terms = mesh.devices.shape
    inner_size = math.isqrt(blocks)
    grid = Mesh(mesh.devices.reshape(blocks // inner_size, inner_size, terms), ("y", "z", "mpo"))
    blk = ("y", "z")
    in_specs = (
        P(blk, None, None),
        P("mpo", blk, None, None),
        P("mpo", blk, None, None),
        P(blk, None),
        P(),
    )
    out_specs = P(blk, None, "mpo")
    return jax.shard_map(local, mesh=grid, in_specs=in_specs, out_specs=out_specs, check_vma=False)
```

```python
import math

import jax
import jax.numpy as jnp
from jax import lax
from jax.sharding import Mesh
from jax.sharding import PartitionSpec as P


def local(wave, left_env, right_env, right_sector, right_home):
    terms = lax.axis_size("mpo")
    inner_size = lax.axis_size("z")
    size = wave.shape[1]
    width = size // terms
    own = right_env[0, 0].reshape(1, terms, width, size)
    spread = jnp.broadcast_to(own, (inner_size, terms, width, size)).reshape(inner_size * terms, width, size)
    row = lax.all_to_all(spread, ("z", "mpo"), 0, 0, tiled=True)
    table = lax.all_gather(row, "y", axis=0, tiled=False)
    table = table.reshape(-1, terms * width, size)
    lefts = lax.all_gather(left_env[0, 0], "mpo", axis=0, tiled=False)
    places = jnp.take(right_home, right_sector[:, 0], axis=0)
    blocks = wave.shape[0]
    rows = table.shape[0]
    cap = 2
    order = jnp.arange(blocks)
    rank = jnp.sum((places[:, None] == places[None, :]) & (order[:, None] > order[None, :]), axis=1)
    slot = places * cap + rank
    owner = jnp.full((rows * cap,), blocks, jnp.int32).at[slot].set(order.astype(jnp.int32))
    slotted = jnp.take(wave, owner, axis=0, mode="clip").reshape(rows, cap, size, size)
    inner = jnp.einsum("prk,psjk->psrj", table, slotted, preferred_element_type=jnp.float32)
    inner = inner.astype(jnp.bfloat16).reshape(rows, cap, terms, width, size)
    out = jnp.einsum("pswcj,wij->psci", inner, lefts, preferred_element_type=jnp.float32)
    out = jnp.take(out.astype(jnp.bfloat16).reshape(rows * cap, width, size), slot, axis=0, mode="clip")
    return jnp.swapaxes(out, 1, 2)


def solution(mesh):
    blocks, terms = mesh.devices.shape
    inner_size = math.isqrt(blocks)
    grid = Mesh(mesh.devices.reshape(blocks // inner_size, inner_size, terms), ("y", "z", "mpo"))
    blk = ("y", "z")
    in_specs = (
        P(blk, None, None),
        P("mpo", blk, None, None),
        P("mpo", blk, None, None),
        P(blk, None),
        P(),
    )
    out_specs = P(blk, None, "mpo")
    return jax.shard_map(local, mesh=grid, in_specs=in_specs, out_specs=out_specs, check_vma=False)
```

```python
import math

import jax
import jax.numpy as jnp
from jax import lax
from jax.sharding import Mesh
from jax.sharding import PartitionSpec as P


def local(wave, left_env, right_env, right_sector, right_home):
    terms = lax.axis_size("mpo")
    inner_size = lax.axis_size("z")
    size = wave.shape[1]
    width = size // terms
    own = right_env[0, 0].reshape(1, terms, width, size)
    spread = jnp.broadcast_to(own, (inner_size, terms, width, size)).reshape(inner_size * terms, width, size)
    row = lax.all_to_all(spread, ("z", "mpo"), 0, 0, tiled=True)
    table = lax.all_gather(row, "y", axis=0, tiled=False)
    table = table.reshape(-1, terms * width, size)
    lefts = lax.all_gather(left_env[0, 0], "mpo", axis=0, tiled=False)
    places = jnp.take(right_home, right_sector[:, 0], axis=0)
    blocks = wave.shape[0]
    rows = table.shape[0]
    cap = 2
    order = jnp.arange(blocks)
    rank = jnp.sum((places[:, None] == places[None, :]) & (order[:, None] > order[None, :]), axis=1)
    slot = places * cap + rank
    owner = jnp.full((rows * cap,), blocks, jnp.int32).at[slot].set(order.astype(jnp.int32))
    slotted = jnp.take(wave, owner, axis=0, mode="clip").reshape(rows, cap, size, size)
    inner = jnp.einsum("prk,psjk->psrj", table, slotted, preferred_element_type=jnp.float32)
    inner = inner.astype(jnp.bfloat16).reshape(rows, cap, terms, width, size)
    out = jnp.einsum("pswcj,wij->psci", inner, lefts, preferred_element_type=jnp.float32)
    out = out.astype(jnp.bfloat16).reshape(rows * cap, width * size)
    pick = (slot[:, None] == jnp.arange(rows * cap)[None, :]).astype(jnp.bfloat16)
    out = jnp.dot(pick, out, preferred_element_type=jnp.float32).astype(jnp.bfloat16)
    return jnp.swapaxes(out.reshape(blocks, width, size), 1, 2)


def solution(mesh):
    blocks, terms = mesh.devices.shape
    inner_size = math.isqrt(blocks)
    grid = Mesh(mesh.devices.reshape(blocks // inner_size, inner_size, terms), ("y", "z", "mpo"))
    blk = ("y", "z")
    in_specs = (
        P(blk, None, None),
        P("mpo", blk, None, None),
        P("mpo", blk, None, None),
        P(blk, None),
        P(),
    )
    out_specs = P(blk, None, "mpo")
    return jax.shard_map(local, mesh=grid, in_specs=in_specs, out_specs=out_specs, check_vma=False)
```

```python
import math

import jax
import jax.numpy as jnp
from jax import lax
from jax.sharding import Mesh
from jax.sharding import PartitionSpec as P


def local(wave, left_env, right_env, right_sector, right_home):
    terms = lax.axis_size("mpo")
    inner_size = lax.axis_size("z")
    size = wave.shape[1]
    width = size // terms
    own = right_env[0, 0].reshape(1, terms, width, size)
    outer_size = lax.axis_size("y")
    spread = jnp.broadcast_to(own, (outer_size, terms, width, size)).reshape(outer_size * terms, width, size)
    row = lax.all_to_all(spread, ("y", "mpo"), 0, 0, tiled=True)
    table = lax.all_gather(row, "z", axis=0, tiled=False)
    table = table.reshape(-1, terms * width, size)
    lefts = lax.all_gather(left_env[0, 0], "mpo", axis=0, tiled=False)
    places = jnp.take(right_home, right_sector[:, 0], axis=0)
    places = (places % inner_size) * outer_size + places // inner_size
    blocks = wave.shape[0]
    rows = table.shape[0]
    cap = 2
    order = jnp.arange(blocks)
    rank = jnp.sum((places[:, None] == places[None, :]) & (order[:, None] > order[None, :]), axis=1)
    slot = places * cap + rank
    owner = jnp.full((rows * cap,), blocks, jnp.int32).at[slot].set(order.astype(jnp.int32))
    slotted = jnp.take(wave, owner, axis=0, mode="clip").reshape(rows, cap, size, size)
    inner = jnp.einsum("prk,psjk->psrj", table, slotted, preferred_element_type=jnp.float32)
    inner = inner.astype(jnp.bfloat16).reshape(rows, cap, terms, width, size)
    out = jnp.einsum("pswcj,wij->psci", inner, lefts, preferred_element_type=jnp.float32)
    out = out.astype(jnp.bfloat16).reshape(rows * cap, width * size)
    pick = (slot[:, None] == jnp.arange(rows * cap)[None, :]).astype(jnp.bfloat16)
    out = jnp.dot(pick, out, preferred_element_type=jnp.float32).astype(jnp.bfloat16)
    return jnp.swapaxes(out.reshape(blocks, width, size), 1, 2)


def solution(mesh):
    blocks, terms = mesh.devices.shape
    inner_size = math.isqrt(blocks)
    grid = Mesh(mesh.devices.reshape(blocks // inner_size, inner_size, terms), ("y", "z", "mpo"))
    blk = ("y", "z")
    in_specs = (
        P(blk, None, None),
        P("mpo", blk, None, None),
        P("mpo", blk, None, None),
        P(blk, None),
        P(),
    )
    out_specs = P(blk, None, "mpo")
    return jax.shard_map(local, mesh=grid, in_specs=in_specs, out_specs=out_specs, check_vma=False)
```

```python
import math

import jax
import jax.numpy as jnp
from jax import lax
from jax.sharding import Mesh
from jax.sharding import PartitionSpec as P


def local(wave, left_env, right_env, right_sector, right_home):
    terms = lax.axis_size(("x", "c"))
    inner_size = lax.axis_size("z")
    size = wave.shape[1]
    width = size // terms
    cores = lax.axis_size("c")
    core = lax.axis_index("c")
    own = right_env[0, 0].reshape(terms // cores, cores, width, size)
    keep = jnp.where(core == 0, own[:, 0], own[:, 1])
    give = jnp.where(core == 0, own[:, 1], own[:, 0])
    got = lax.ppermute(give, "c", [(0, 1), (1, 0)])
    pair = jnp.where(core == 0, jnp.stack([keep, got], 1), jnp.stack([got, keep], 1))
    spread = jnp.broadcast_to(pair[None], (inner_size,) + pair.shape).reshape(-1, cores, width, size)
    row = lax.all_to_all(spread, ("z", "x"), 0, 0, tiled=True)
    table = lax.all_gather(row, "y", axis=0, tiled=False)
    table = table.reshape(-1, terms * width, size)
    lefts = lax.all_gather(left_env[0, 0], ("x", "c"), axis=0, tiled=False)
    places = jnp.take(right_home, right_sector[:, 0], axis=0)
    blocks = wave.shape[0]
    rows = table.shape[0]
    cap = 2
    order = jnp.arange(blocks)
    rank = jnp.sum((places[:, None] == places[None, :]) & (order[:, None] > order[None, :]), axis=1)
    slot = places * cap + rank
    owner = jnp.full((rows * cap,), blocks, jnp.int32).at[slot].set(order.astype(jnp.int32))
    slotted = jnp.take(wave, owner, axis=0, mode="clip").reshape(rows, cap, size, size)
    inner = jnp.einsum("prk,psjk->psrj", table, slotted, preferred_element_type=jnp.float32)
    inner = inner.astype(jnp.bfloat16).reshape(rows, cap, terms, width, size)
    out = jnp.einsum("pswcj,wij->psci", inner, lefts, preferred_element_type=jnp.float32)
    out = out.astype(jnp.bfloat16).reshape(rows * cap, width * size)
    pick = (slot[:, None] == jnp.arange(rows * cap)[None, :]).astype(jnp.bfloat16)
    out = jnp.dot(pick, out, preferred_element_type=jnp.float32).astype(jnp.bfloat16)
    return jnp.swapaxes(out.reshape(blocks, width, size), 1, 2)


def solution(mesh):
    blocks, terms = mesh.devices.shape
    inner_size = math.isqrt(blocks)
    grid = Mesh(mesh.devices.reshape(blocks // inner_size, inner_size, terms // 2, 2), ("y", "z", "x", "c"))
    blk = ("y", "z")
    mpo = ("x", "c")
    in_specs = (
        P(blk, None, None),
        P(mpo, blk, None, None),
        P(mpo, blk, None, None),
        P(blk, None),
        P(),
    )
    out_specs = P(blk, None, mpo)
    return jax.shard_map(local, mesh=grid, in_specs=in_specs, out_specs=out_specs, check_vma=False)
```

```python
import math

import jax
import jax.numpy as jnp
from jax import lax
from jax.sharding import Mesh
from jax.sharding import PartitionSpec as P


def local(wave, left_env, right_env, right_sector, right_home):
    terms = lax.axis_size("mpo")
    inner_size = lax.axis_size("z")
    size = wave.shape[1]
    width = size // terms
    own = right_env[0, 0].reshape(terms, 1, width, size)
    spread = jnp.broadcast_to(own, (terms, inner_size, width, size)).reshape(terms * inner_size, width, size)
    row = lax.all_to_all(spread, ("mpo", "z"), 0, 0, tiled=True)
    row = jnp.swapaxes(row.reshape(terms, inner_size, width, size), 0, 1).reshape(-1, width, size)
    table = lax.all_gather(row, "y", axis=0, tiled=False)
    table = table.reshape(-1, terms * width, size)
    lefts = lax.all_gather(left_env[0, 0], "mpo", axis=0, tiled=False)
    places = jnp.take(right_home, right_sector[:, 0], axis=0)
    blocks = wave.shape[0]
    rows = table.shape[0]
    cap = 2
    order = jnp.arange(blocks)
    rank = jnp.sum((places[:, None] == places[None, :]) & (order[:, None] > order[None, :]), axis=1)
    slot = places * cap + rank
    owner = jnp.full((rows * cap,), blocks, jnp.int32).at[slot].set(order.astype(jnp.int32))
    slotted = jnp.take(wave, owner, axis=0, mode="clip").reshape(rows, cap, size, size)
    inner = jnp.einsum("prk,psjk->psrj", table, slotted, preferred_element_type=jnp.float32)
    inner = inner.astype(jnp.bfloat16).reshape(rows, cap, terms, width, size)
    out = jnp.einsum("pswcj,wij->psci", inner, lefts, preferred_element_type=jnp.float32)
    out = out.astype(jnp.bfloat16).reshape(rows * cap, width * size)
    pick = (slot[:, None] == jnp.arange(rows * cap)[None, :]).astype(jnp.bfloat16)
    out = jnp.dot(pick, out, preferred_element_type=jnp.float32).astype(jnp.bfloat16)
    return jnp.swapaxes(out.reshape(blocks, width, size), 1, 2)


def solution(mesh):
    blocks, terms = mesh.devices.shape
    inner_size = math.isqrt(blocks)
    grid = Mesh(mesh.devices.reshape(blocks // inner_size, inner_size, terms), ("y", "z", "mpo"))
    blk = ("y", "z")
    in_specs = (
        P(blk, None, None),
        P("mpo", blk, None, None),
        P("mpo", blk, None, None),
        P(blk, None),
        P(),
    )
    out_specs = P(blk, None, "mpo")
    return jax.shard_map(local, mesh=grid, in_specs=in_specs, out_specs=out_specs, check_vma=False)
```
